32 devices in a mesh: row: 2 (over x), col: 16 (over z, y, core).
Axes of the slice: x: 2, y: 2, z: 4, core: 2. Of those that a mesh axis runs over, the one named last changes fastest.
Arguments:
- source: float32 [48, 1536, 1536], P('row', 'col'), may hold values from -16 to 16
- lower_coef: float32 [48], replicated, may hold values from 0.004 to 18, as said below
- upper_coef: float32 [48], replicated, may hold values from 0.004 to 18, as said below
Outputs:
- pressure: float32 [48, 1536, 1536], P('row', 'col')
The draws below stay inside these ranges and needn't reach their ends.
Inputs may be any that keep to these rules, and one draw needn't show every extreme that they name: lower_coef[z] = 2 / (h[z] (h[z] + h[z-1])) and upper_coef[z] = 2 / (h[z] (h[z] + h[z+1])) for positive level thicknesses h shared by both, with h[-1] = h[0]. `upper_coef`: the same thicknesses as for lower_coef, with h[48] = h[47].
All inputs are finite; a program needn't handle non-finite values.
Results may differ from the reference program's by a relative error of at most 0.0018.
Values sent between devices are 32-bit elements; how exact they have to be, the bound alone decides.
No kernel may reach another device: no remote copies, remote signals or barrier semaphores. Data moves between devices by JAX's collectives and lax.ppermute only.
A program may use at most 192 MiB of HBM per device.

```python
import math
import jax
import jax.numpy as jnp
from jax import lax

NX = 1536
NY = 1536
NZ = 48


def level_thickness(key):
    grid_key = jax.random.fold_in(key, 5)
    first_key, second_key, third_key = jax.random.split(grid_key, 3)
    bottom_thickness = jax.random.uniform(first_key, (), jnp.float32, 0.3, 0.6)
    stretch = jax.random.uniform(second_key, (), jnp.float32, 1.02, 1.06)
    roughness = jnp.exp(jax.random.uniform(third_key, (NZ,), jnp.float32, math.log(0.8), math.log(1.6)))
    level_index = lax.iota(jnp.float32, NZ)
    return bottom_thickness * stretch ** level_index * roughness


def draw_lower_coef(key, part):
    thickness = level_thickness(key)
    thick_below = jnp.concatenate([thickness[:1], thickness[:-1]], axis=0)
    return (2.0 / (thickness * (thickness + thick_below))).astype(jnp.float32)


def draw_upper_coef(key, part):
    thickness = level_thickness(key)
    thick_above = jnp.concatenate([thickness[1:], thickness[-1:]], axis=0)
    return (2.0 / (thickness * (thickness + thick_above))).astype(jnp.float32)


def draw_source(key, part):
    flow_key = jax.random.fold_in(key, 11)
    first_key, second_key = jax.random.split(flow_key, 2)
    velocity_x = jnp.clip(jax.random.normal(first_key, (NZ, NY, NX), jnp.float32), -4.0, 4.0)
    velocity_y = jnp.clip(jax.random.normal(second_key, (NZ, NY, NX), jnp.float32), -4.0, 4.0)
    divergence = jnp.roll(velocity_x, -1, axis=2) - velocity_x + (jnp.roll(velocity_y, -1, axis=1) - velocity_y)
    return divergence.astype(jnp.float32)


def setup_inputs(seed: int = 0) -> dict:
    seeds = jax.random.split(jax.random.key(seed), 4)
    return {
        "source": draw_source(jax.random.fold_in(seeds[3], 71), 0),
        "lower_coef": draw_lower_coef(jax.random.fold_in(seeds[3], 71), 0),
        "upper_coef": draw_upper_coef(jax.random.fold_in(seeds[3], 71), 0),
    }


def hartley(values, axis):
    spectrum = jnp.fft.fft(values, axis=axis)
    return (jnp.real(spectrum) - jnp.imag(spectrum)).astype(values.dtype)


def eigen_values(wave_index, length):
    return 2.0 * jnp.cos(wave_index.astype(jnp.float32) * (2.0 * math.pi / length)) - 2.0


def vertical_solve(spectra, lower_coef, upper_coef, eigen_sum, pinned):
    levels = spectra.shape[0]
    level_index = lax.iota(jnp.int32, levels)
    below = jnp.where(level_index > 0, lower_coef, 0.0)
    above = jnp.where(level_index < levels - 1, upper_coef, 0.0)
    head_diag = jnp.where(pinned, 1.0, eigen_sum - above[0])
    head_upper = jnp.where(pinned, 0.0, above[0])
    head_right = jnp.where(pinned, 0.0, spectra[0])
    start = (head_upper / head_diag, head_right / head_diag)

    def forward(carry, item):
        ratio_before, value_before = carry
        low_coef, high_coef, right_side = item
        pivot = eigen_sum - low_coef - high_coef - low_coef * ratio_before
        ratio_next = high_coef / pivot
        value_next = (right_side - low_coef * value_before) / pivot
        return (ratio_next, value_next), (ratio_next, value_next)

    unused, (ratios, values) = lax.scan(forward, start, (below[1:], above[1:], spectra[1:]))
    ratios = jnp.concatenate([start[0][None], ratios], axis=0)
    values = jnp.concatenate([start[1][None], values], axis=0)

    def backward(later, item):
        ratio_here, value_here = item
        result = value_here - ratio_here * later
        return result, result

    unused, solved = lax.scan(backward, jnp.zeros_like(eigen_sum), (ratios, values), reverse=True)
    return solved


def reference(source, lower_coef, upper_coef):
    spectra = hartley(hartley(source, 2), 1)
    wave_y = lax.iota(jnp.int32, NY)
    wave_x = lax.iota(jnp.int32, NX)
    eigen_sum = eigen_values(wave_y, NY)[:, None] + eigen_values(wave_x, NX)[None, :]
    pinned = (wave_y == 0)[:, None] & (wave_x == 0)[None, :]
    solved = vertical_solve(spectra, lower_coef, upper_coef, eigen_sum, pinned)
    pressure = hartley(hartley(solved, 1), 2) * (1.0 / (NX * NY))
    return pressure.astype(jnp.float32)
```

```python
import math

import jax
import jax.numpy as jnp
from jax import lax
from jax.sharding import PartitionSpec as P
from jax.experimental import pallas as pl
from jax.experimental.pallas import tpu as pltpu


def cas_table(row_index, col_index, length):
    product = row_index[:, None] * col_index[None, :] % length
    angles = product.astype(jnp.float32) * (2.0 * math.pi / length)
    return jnp.cos(angles) + jnp.sin(angles)


def eigen_values(wave_index, length):
    return 2.0 * jnp.cos(wave_index.astype(jnp.float32) * (2.0 * math.pi / length)) - 2.0


def solve_kernel(lower_ref, upper_ref, eigen_ref, pinned_ref, spectra_ref, solved_ref, ratio_ref):
    levels = spectra_ref.shape[0]
    eigen_sum = eigen_ref[...]
    pinned = pinned_ref[...] > 0.5
    above_first = upper_ref[0]
    head_diag = jnp.where(pinned, 1.0, eigen_sum - above_first)
    head_upper = jnp.where(pinned, 0.0, above_first)
    head_right = jnp.where(pinned, 0.0, spectra_ref[0])
    ratio_ref[0] = head_upper / head_diag
    solved_ref[0] = head_right / head_diag

    def forward(level, carry):
        ratio_before, value_before = carry
        low_coef = lower_ref[level]
        high_coef = jnp.where(level < levels - 1, upper_ref[level], 0.0)
        pivot = eigen_sum - low_coef - high_coef - low_coef * ratio_before
        ratio_next = high_coef / pivot
        value_next = (spectra_ref[level] - low_coef * value_before) / pivot
        ratio_ref[level] = ratio_next
        solved_ref[level] = value_next
        return ratio_next, value_next

    unused, last = lax.fori_loop(1, levels, forward, (ratio_ref[0], solved_ref[0]))

    def backward(step, later):
        level = levels - 2 - step
        result = solved_ref[level] - ratio_ref[level] * later
        solved_ref[level] = result
        return result

    lax.fori_loop(0, levels - 1, backward, last)


def vertical_solve(spectra, lower_coef, upper_coef, eigen_sum, pinned):
    levels, part_x, part_y = spectra.shape
    block = 8 if part_x % 8 == 0 else part_x
    column_spec = pl.BlockSpec((levels, block, part_y), lambda i: (0, i, 0))
    plane_spec = pl.BlockSpec((block, part_y), lambda i: (i, 0))
    scalar_spec = pl.BlockSpec(memory_space=pltpu.SMEM)
    return pl.pallas_call(
        solve_kernel,
        grid=(part_x // block,),
        in_specs=[scalar_spec, scalar_spec, plane_spec, plane_spec, column_spec],
        out_specs=column_spec,
        out_shape=jax.ShapeDtypeStruct(spectra.shape, jnp.float32),
        scratch_shapes=[pltpu.VMEM((levels, block, part_y), jnp.float32)],
    )(lower_coef, upper_coef, eigen_sum, pinned.astype(jnp.float32), spectra)


def body(source, lower_coef, upper_coef):
    highest = lax.Precision.HIGHEST
    slab_levels, slab_rows, full_x = source.shape
    col_count = lax.axis_size("col")
    full_y = slab_rows * col_count
    index_x = lax.iota(jnp.int32, full_x)
    index_y = lax.iota(jnp.int32, full_y)
    table_x = cas_table(index_x, index_x, full_x)
    table_y = cas_table(index_y, index_y, full_y)
    along_x = jnp.einsum("zyx,xk->zky", source, table_x, precision=highest)
    scale = 1.0 / (full_x * full_y)
    spectra = jnp.einsum(
        "zxy,yk->zxk",
        lax.all_to_all(along_x, "col", split_axis=1, concat_axis=2, tiled=True),
        table_y,
        precision=highest,
    )
    columns = lax.all_to_all(spectra, "row", split_axis=2, concat_axis=0, tiled=True)
    part_x = columns.shape[1]
    part_y = columns.shape[2]
    wave_x = lax.axis_index("col") * part_x + lax.iota(jnp.int32, part_x)
    wave_y = lax.axis_index("row") * part_y + lax.iota(jnp.int32, part_y)
    eigen_sum = eigen_values(wave_x, full_x)[:, None] + eigen_values(wave_y, full_y)[None, :]
    pinned = (wave_x == 0)[:, None] & (wave_y == 0)[None, :]
    solved = vertical_solve(columns, lower_coef, upper_coef, eigen_sum, pinned)
    returned = lax.all_to_all(solved, "row", split_axis=0, concat_axis=2, tiled=True)
    inverse_y = jnp.einsum("zxk,ky->zxy", returned, table_y, precision=highest)
    pressure = jnp.einsum(
        "zky,kn->zyn",
        lax.all_to_all(inverse_y, "col", split_axis=2, concat_axis=1, tiled=True),
        table_x,
        precision=highest,
    )
    return pressure * scale


def solution(mesh):
    placed = (P("row", "col", None), P(), P())
    return jax.shard_map(
        body, mesh=mesh, in_specs=placed, out_specs=P("row", "col", None), check_vma=False
    )
```

```python
import math

import numpy as np

import jax
import jax.numpy as jnp
from jax import lax
from jax.sharding import PartitionSpec as P
from jax.experimental import pallas as pl
from jax.experimental.pallas import tpu as pltpu


def cas_table(row_index, col_index, length):
    product = row_index[:, None] * col_index[None, :] % length
    angles = product.astype(jnp.float32) * (2.0 * math.pi / length)
    return jnp.cos(angles) + jnp.sin(angles)


def cas_constant(row_index, col_index, length):
    product = np.outer(row_index, col_index) % length
    angles = product.astype(np.float64) * (2.0 * math.pi / length)
    return jnp.asarray((np.cos(angles) + np.sin(angles)).astype(np.float32))


def eigen_values(wave_index, length):
    return 2.0 * jnp.cos(wave_index.astype(jnp.float32) * (2.0 * math.pi / length)) - 2.0


def solve_kernel(lower_ref, upper_ref, eigen_ref, pinned_ref, spectra_ref, solved_ref, ratio_ref):
    levels = spectra_ref.shape[0]
    eigen_sum = eigen_ref[...]
    pinned = pinned_ref[...] > 0.5
    above_first = upper_ref[0]
    head_diag = jnp.where(pinned, 1.0, eigen_sum - above_first)
    head_upper = jnp.where(pinned, 0.0, above_first)
    head_right = jnp.where(pinned, 0.0, spectra_ref[0])
    ratio_ref[0] = head_upper / head_diag
    solved_ref[0] = head_right / head_diag

    def forward(level, carry):
        ratio_before, value_before = carry
        low_coef = lower_ref[level]
        high_coef = jnp.where(level < levels - 1, upper_ref[level], 0.0)
        pivot = eigen_sum - low_coef - high_coef - low_coef * ratio_before
        ratio_next = high_coef / pivot
        value_next = (spectra_ref[level] - low_coef * value_before) / pivot
        ratio_ref[level] = ratio_next
        solved_ref[level] = value_next
        return ratio_next, value_next

    unused, last = lax.fori_loop(1, levels, forward, (ratio_ref[0], solved_ref[0]))

    def backward(step, later):
        level = levels - 2 - step
        result = solved_ref[level] - ratio_ref[level] * later
        solved_ref[level] = result
        return result

    lax.fori_loop(0, levels - 1, backward, last)


def vertical_solve(spectra, lower_coef, upper_coef, eigen_sum, pinned):
    levels, part_x, part_y = spectra.shape
    block = 8 if part_x % 8 == 0 else part_x
    column_spec = pl.BlockSpec((levels, block, part_y), lambda i: (0, i, 0))
    plane_spec = pl.BlockSpec((block, part_y), lambda i: (i, 0))
    scalar_spec = pl.BlockSpec(memory_space=pltpu.SMEM)
    return pl.pallas_call(
        solve_kernel,
        grid=(part_x // block,),
        in_specs=[scalar_spec, scalar_spec, plane_spec, plane_spec, column_spec],
        out_specs=column_spec,
        out_shape=jax.ShapeDtypeStruct(spectra.shape, jnp.float32),
        scratch_shapes=[pltpu.VMEM((levels, block, part_y), jnp.float32)],
    )(lower_coef, upper_coef, eigen_sum, pinned.astype(jnp.float32), spectra)


def body(source, lower_coef, upper_coef, chunks=4):
    highest = lax.Precision.HIGHEST
    slab_levels, slab_rows, full_x = source.shape
    col_count = lax.axis_size("col")
    full_y = slab_rows * col_count
    part_x = full_x // col_count
    chunk_x = part_x // chunks
    index_x = np.arange(full_x)
    table_y = cas_constant(np.arange(full_y), np.arange(full_y), full_y)
    scale = 1.0 / (full_x * full_y)
    pressure = None
    for chunk in range(chunks):
        waves = (np.arange(col_count)[:, None] * part_x + chunk * chunk_x
                 + np.arange(chunk_x)[None, :]).reshape(-1)
        table_chunk = cas_constant(index_x, waves, full_x)
        table_back = cas_constant(waves, index_x, full_x)
        along_x = jnp.einsum("zyx,xk->zky", source, table_chunk, precision=highest)
        spectra = jnp.einsum(
            "zxy,yk->zxk",
            lax.all_to_all(along_x, "col", split_axis=1, concat_axis=2, tiled=True),
            table_y,
            precision=highest,
        )
        columns = lax.all_to_all(spectra, "row", split_axis=2, concat_axis=0, tiled=True)
        part_y = columns.shape[2]
        wave_x = lax.axis_index("col") * part_x + chunk * chunk_x + lax.iota(jnp.int32, chunk_x)
        wave_y = lax.axis_index("row") * part_y + lax.iota(jnp.int32, part_y)
        eigen_sum = eigen_values(wave_x, full_x)[:, None] + eigen_values(wave_y, full_y)[None, :]
        pinned = (wave_x == 0)[:, None] & (wave_y == 0)[None, :]
        solved = vertical_solve(columns, lower_coef, upper_coef, eigen_sum, pinned)
        returned = lax.all_to_all(solved, "row", split_axis=0, concat_axis=2, tiled=True)
        inverse_y = jnp.einsum("zxk,ky->zxy", returned, table_y, precision=highest)
        part = jnp.einsum(
            "zky,kn->zyn",
            lax.all_to_all(inverse_y, "col", split_axis=2, concat_axis=1, tiled=True),
            table_back,
            precision=highest,
        )
        pressure = part if pressure is None else pressure + part
    return pressure * scale


def solution(mesh):
    placed = (P("row", "col", None), P(), P())
    return jax.shard_map(
        body, mesh=mesh, in_specs=placed, out_specs=P("row", "col", None), check_vma=False
    )
```

```python
import math

import numpy as np

import jax
import jax.numpy as jnp
from jax import lax
from jax.sharding import PartitionSpec as P
from jax.experimental import pallas as pl
from jax.experimental.pallas import tpu as pltpu


def cas_table(row_index, col_index, length):
    product = row_index[:, None] * col_index[None, :] % length
    angles = product.astype(jnp.float32) * (2.0 * math.pi / length)
    return jnp.cos(angles) + jnp.sin(angles)


def cas_constant(row_index, col_index, length):
    product = np.outer(row_index, col_index) % length
    angles = product.astype(np.float64) * (2.0 * math.pi / length)
    return jnp.asarray((np.cos(angles) + np.sin(angles)).astype(np.float32))


def eigen_values(wave_index, length):
    return 2.0 * jnp.cos(wave_index.astype(jnp.float32) * (2.0 * math.pi / length)) - 2.0


def solve_kernel(lower_ref, upper_ref, eigen_ref, pinned_ref, spectra_ref, solved_ref, ratio_ref):
    levels = spectra_ref.shape[0]
    eigen_sum = eigen_ref[...]
    pinned = pinned_ref[...] > 0.5
    above_first = upper_ref[0]
    head_diag = jnp.where(pinned, 1.0, eigen_sum - above_first)
    head_upper = jnp.where(pinned, 0.0, above_first)
    head_right = jnp.where(pinned, 0.0, spectra_ref[0])
    ratio_ref[0] = head_upper / head_diag
    solved_ref[0] = head_right / head_diag

    def forward(level, carry):
        ratio_before, value_before = carry
        low_coef = lower_ref[level]
        high_coef = jnp.where(level < levels - 1, upper_ref[level], 0.0)
        pivot = eigen_sum - low_coef - high_coef - low_coef * ratio_before
        ratio_next = high_coef / pivot
        value_next = (spectra_ref[level] - low_coef * value_before) / pivot
        ratio_ref[level] = ratio_next
        solved_ref[level] = value_next
        return ratio_next, value_next

    unused, last = lax.fori_loop(1, levels, forward, (ratio_ref[0], solved_ref[0]))

    def backward(step, later):
        level = levels - 2 - step
        result = solved_ref[level] - ratio_ref[level] * later
        solved_ref[level] = result
        return result

    lax.fori_loop(0, levels - 1, backward, last)


def vertical_solve(spectra, lower_coef, upper_coef, eigen_sum, pinned):
    levels, part_x, part_y = spectra.shape
    block = 8 if part_x % 8 == 0 else part_x
    column_spec = pl.BlockSpec((levels, block, part_y), lambda i: (0, i, 0))
    plane_spec = pl.BlockSpec((block, part_y), lambda i: (i, 0))
    scalar_spec = pl.BlockSpec(memory_space=pltpu.SMEM)
    return pl.pallas_call(
        solve_kernel,
        grid=(part_x // block,),
        in_specs=[scalar_spec, scalar_spec, plane_spec, plane_spec, column_spec],
        out_specs=column_spec,
        out_shape=jax.ShapeDtypeStruct(spectra.shape, jnp.float32),
        scratch_shapes=[pltpu.VMEM((levels, block, part_y), jnp.float32)],
    )(lower_coef, upper_coef, eigen_sum, pinned.astype(jnp.float32), spectra)


def body(source, lower_coef, upper_coef, chunks=4):
    highest = lax.Precision.HIGHEST
    slab_levels, slab_rows, full_x = source.shape
    col_count = lax.axis_size("col")
    row_count = lax.axis_size("row")
    full_y = slab_rows * col_count
    part_x = full_x // col_count
    part_y = full_y // row_count
    chunk_x = part_x // chunks
    index_x = np.arange(full_x)
    table_y = cas_constant(np.arange(full_y), np.arange(full_y), full_y)
    forward_y = table_y.reshape(col_count, slab_rows, row_count, part_y)
    inverse_y = table_y.reshape(row_count, part_y, col_count, slab_rows)
    scale = 1.0 / (full_x * full_y)
    wave_y = lax.axis_index("row") * part_y + lax.iota(jnp.int32, part_y)
    pressure = None
    for chunk in range(chunks):
        waves = (np.arange(col_count)[:, None] * part_x + chunk * chunk_x
                 + np.arange(chunk_x)[None, :]).reshape(-1)
        table_chunk = cas_constant(index_x, waves, full_x).reshape(full_x, col_count, chunk_x)
        table_back = cas_constant(waves, index_x, full_x).reshape(col_count, chunk_x, full_x)
        along_x = jnp.einsum("zyx,xdi->dziy", source, table_chunk, precision=highest)
        gathered = lax.all_to_all(along_x, "col", 0, 0, tiled=True)
        spectra = jnp.einsum("sziy,syhj->hzij", gathered, forward_y, precision=highest)
        columns = lax.all_to_all(spectra, "row", 0, 0, tiled=True)
        columns = columns.reshape(row_count * slab_levels, chunk_x, part_y)
        wave_x = lax.axis_index("col") * part_x + chunk * chunk_x + lax.iota(jnp.int32, chunk_x)
        eigen_sum = eigen_values(wave_x, full_x)[:, None] + eigen_values(wave_y, full_y)[None, :]
        pinned = (wave_x == 0)[:, None] & (wave_y == 0)[None, :]
        solved = vertical_solve(columns, lower_coef, upper_coef, eigen_sum, pinned)
        solved = solved.reshape(row_count, slab_levels, chunk_x, part_y)
        returned = lax.all_to_all(solved, "row", 0, 0, tiled=True)
        back_y = jnp.einsum("hzij,hjsy->sziy", returned, inverse_y, precision=highest)
        scattered = lax.all_to_all(back_y, "col", 0, 0, tiled=True)
        part = jnp.einsum("dziy,din->zyn", scattered, table_back, precision=highest)
        pressure = part if pressure is None else pressure + part
    return pressure * scale


def solution(mesh):
    placed = (P("row", "col", None), P(), P())
    return jax.shard_map(
        body, mesh=mesh, in_specs=placed, out_specs=P("row", "col", None), check_vma=False
    )
```

```python
import math

import numpy as np

import jax
import jax.numpy as jnp
from jax import lax
from jax.sharding import PartitionSpec as P
from jax.experimental import pallas as pl
from jax.experimental.pallas import tpu as pltpu


def cas_table(row_index, col_index, length):
    product = row_index[:, None] * col_index[None, :] % length
    angles = product.astype(jnp.float32) * (2.0 * math.pi / length)
    return jnp.cos(angles) + jnp.sin(angles)


def cas_constant(row_index, col_index, length):
    product = np.outer(row_index, col_index) % length
    angles = product.astype(np.float64) * (2.0 * math.pi / length)
    return jnp.asarray((np.cos(angles) + np.sin(angles)).astype(np.float32))


def eigen_values(wave_index, length):
    return 2.0 * jnp.cos(wave_index.astype(jnp.float32) * (2.0 * math.pi / length)) - 2.0


def solve_kernel(lower_ref, upper_ref, eigen_ref, pinned_ref, spectra_ref, solved_ref, ratio_ref):
    levels = spectra_ref.shape[0]
    eigen_sum = eigen_ref[...]
    pinned = pinned_ref[...] > 0.5
    above_first = upper_ref[0]
    head_diag = jnp.where(pinned, 1.0, eigen_sum - above_first)
    head_upper = jnp.where(pinned, 0.0, above_first)
    head_right = jnp.where(pinned, 0.0, spectra_ref[0])
    ratio_ref[0] = head_upper / head_diag
    solved_ref[0] = head_right / head_diag

    def forward(level, carry):
        ratio_before, value_before = carry
        low_coef = lower_ref[level]
        high_coef = jnp.where(level < levels - 1, upper_ref[level], 0.0)
        pivot = eigen_sum - low_coef - high_coef - low_coef * ratio_before
        ratio_next = high_coef / pivot
        value_next = (spectra_ref[level] - low_coef * value_before) / pivot
        ratio_ref[level] = ratio_next
        solved_ref[level] = value_next
        return ratio_next, value_next

    unused, last = lax.fori_loop(1, levels, forward, (ratio_ref[0], solved_ref[0]))

    def backward(step, later):
        level = levels - 2 - step
        result = solved_ref[level] - ratio_ref[level] * later
        solved_ref[level] = result
        return result

    lax.fori_loop(0, levels - 1, backward, last)


def vertical_solve(spectra, lower_coef, upper_coef, eigen_sum, pinned):
    levels, part_x, part_y = spectra.shape
    block = 8 if part_x % 8 == 0 else part_x
    column_spec = pl.BlockSpec((levels, block, part_y), lambda i: (0, i, 0))
    plane_spec = pl.BlockSpec((block, part_y), lambda i: (i, 0))
    scalar_spec = pl.BlockSpec(memory_space=pltpu.SMEM)
    return pl.pallas_call(
        solve_kernel,
        grid=(part_x // block,),
        in_specs=[scalar_spec, scalar_spec, plane_spec, plane_spec, column_spec],
        out_specs=column_spec,
        out_shape=jax.ShapeDtypeStruct(spectra.shape, jnp.float32),
        scratch_shapes=[pltpu.VMEM((levels, block, part_y), jnp.float32)],
    )(lower_coef, upper_coef, eigen_sum, pinned.astype(jnp.float32), spectra)


def body(source, lower_coef, upper_coef, chunks=4):
    highest = lax.Precision.HIGHEST
    slab_levels, slab_rows, full_x = source.shape
    col_count = lax.axis_size("col")
    row_count = lax.axis_size("row")
    full_y = slab_rows * col_count
    part_x = full_x // col_count
    part_y = full_y // row_count
    chunk_x = part_x // chunks
    index_x = np.arange(full_x)
    table_y = cas_constant(np.arange(full_y), np.arange(full_y), full_y)
    forward_y = table_y.reshape(col_count, slab_rows, row_count, part_y)
    inverse_y = table_y.reshape(row_count, part_y, col_count, slab_rows)
    scale = 1.0 / (full_x * full_y)
    wave_y = lax.axis_index("row") * part_y + lax.iota(jnp.int32, part_y)

    def chunk_waves(chunk):
        return (np.arange(col_count)[:, None] * part_x + chunk * chunk_x
                + np.arange(chunk_x)[None, :]).reshape(-1)

    def along_x(chunk, slab):
        table_chunk = cas_constant(index_x, chunk_waves(chunk), full_x).reshape(full_x, col_count, chunk_x)
        spread = jnp.einsum("zyx,xdi->dziy", slab, table_chunk, precision=highest)
        return lax.all_to_all(spread, "col", 0, 0, tiled=True)

    def middle(chunk, gathered):
        spectra = jnp.einsum("sziy,syhj->hzij", gathered, forward_y, precision=highest)
        columns = lax.all_to_all(spectra, "row", 0, 0, tiled=True)
        columns = columns.reshape(row_count * slab_levels, chunk_x, part_y)
        wave_x = lax.axis_index("col") * part_x + chunk * chunk_x + lax.iota(jnp.int32, chunk_x)
        eigen_sum = eigen_values(wave_x, full_x)[:, None] + eigen_values(wave_y, full_y)[None, :]
        pinned = (wave_x == 0)[:, None] & (wave_y == 0)[None, :]
        solved = vertical_solve(columns, lower_coef, upper_coef, eigen_sum, pinned)
        solved = solved.reshape(row_count, slab_levels, chunk_x, part_y)
        returned = lax.all_to_all(solved, "row", 0, 0, tiled=True)
        return jnp.einsum("hzij,hjsy->sziy", returned, inverse_y, precision=highest)

    def back_x(chunk, back_y):
        table_back = cas_constant(chunk_waves(chunk), index_x, full_x).reshape(col_count, chunk_x, full_x)
        scattered = lax.all_to_all(back_y, "col", 0, 0, tiled=True)
        return jnp.einsum("dziy,din->zyn", scattered, table_back, precision=highest)

    gathered = along_x(0, source)
    gathered, source = lax.optimization_barrier((gathered, source))
    pressure = None
    back_y = None
    for chunk in range(chunks):
        gathered_next = along_x(chunk + 1, source) if chunk + 1 < chunks else None
        if back_y is not None:
            part = back_x(chunk - 1, back_y)
            pressure = part if pressure is None else pressure + part
        back_y = middle(chunk, gathered)
        gathered = gathered_next
        gathered, back_y, pressure, source = lax.optimization_barrier((gathered, back_y, pressure, source))
    part = back_x(chunks - 1, back_y)
    pressure = part if pressure is None else pressure + part
    return pressure * scale


def solution(mesh):
    placed = (P("row", "col", None), P(), P())
    return jax.shard_map(
        body, mesh=mesh, in_specs=placed, out_specs=P("row", "col", None), check_vma=False
    )
```

```python
import math

import numpy as np

import jax
import jax.numpy as jnp
from jax import lax
from jax.sharding import PartitionSpec as P
from jax.experimental import pallas as pl
from jax.experimental.pallas import tpu as pltpu


def cas_table(row_index, col_index, length):
    product = row_index[:, None] * col_index[None, :] % length
    angles = product.astype(jnp.float32) * (2.0 * math.pi / length)
    return jnp.cos(angles) + jnp.sin(angles)


def cas_constant(row_index, col_index, length):
    product = np.outer(row_index, col_index) % length
    angles = product.astype(np.float64) * (2.0 * math.pi / length)
    return jnp.asarray((np.cos(angles) + np.sin(angles)).astype(np.float32))


def eigen_values(wave_index, length):
    return 2.0 * jnp.cos(wave_index.astype(jnp.float32) * (2.0 * math.pi / length)) - 2.0


def solve_kernel(lower_ref, upper_ref, eigen_ref, pinned_ref, spectra_ref, solved_ref, ratio_ref):
    levels = spectra_ref.shape[0]
    eigen_sum = eigen_ref[...]
    pinned = pinned_ref[...] > 0.5
    above_first = upper_ref[0]
    head_diag = jnp.where(pinned, 1.0, eigen_sum - above_first)
    head_upper = jnp.where(pinned, 0.0, above_first)
    head_right = jnp.where(pinned, 0.0, spectra_ref[0])
    ratio_ref[0] = head_upper / head_diag
    solved_ref[0] = head_right / head_diag

    def forward(level, carry):
        ratio_before, value_before = carry
        low_coef = lower_ref[level]
        high_coef = jnp.where(level < levels - 1, upper_ref[level], 0.0)
        pivot = eigen_sum - low_coef - high_coef - low_coef * ratio_before
        ratio_next = high_coef / pivot
        value_next = (spectra_ref[level] - low_coef * value_before) / pivot
        ratio_ref[level] = ratio_next
        solved_ref[level] = value_next
        return ratio_next, value_next

    unused, last = lax.fori_loop(1, levels, forward, (ratio_ref[0], solved_ref[0]))

    def backward(step, later):
        level = levels - 2 - step
        result = solved_ref[level] - ratio_ref[level] * later
        solved_ref[level] = result
        return result

    lax.fori_loop(0, levels - 1, backward, last)


def vertical_solve(spectra, lower_coef, upper_coef, eigen_sum, pinned):
    levels, part_x, part_y = spectra.shape
    block = 8 if part_x % 8 == 0 else part_x
    column_spec = pl.BlockSpec((levels, block, part_y), lambda i: (0, i, 0))
    plane_spec = pl.BlockSpec((block, part_y), lambda i: (i, 0))
    scalar_spec = pl.BlockSpec(memory_space=pltpu.SMEM)
    return pl.pallas_call(
        solve_kernel,
        grid=(part_x // block,),
        in_specs=[scalar_spec, scalar_spec, plane_spec, plane_spec, column_spec],
        out_specs=column_spec,
        out_shape=jax.ShapeDtypeStruct(spectra.shape, jnp.float32),
        scratch_shapes=[pltpu.VMEM((levels, block, part_y), jnp.float32)],
    )(lower_coef, upper_coef, eigen_sum, pinned.astype(jnp.float32), spectra)


def exchange(pieces, axis_name):
    count = pieces.shape[0]
    here = lax.axis_index(axis_name)
    arrived = [lax.dynamic_index_in_dim(pieces, here, keepdims=False)]
    for shift in range(1, count):
        outgoing = lax.dynamic_index_in_dim(pieces, (here + shift) % count, keepdims=False)
        perm = [(device, (device + shift) % count) for device in range(count)]
        arrived.append(lax.ppermute(outgoing, axis_name, perm))
    placed = []
    for source in range(count):
        distance = (here - source) % count
        piece = arrived[0]
        for shift in range(1, count):
            piece = jnp.where(distance == shift, arrived[shift], piece)
        placed.append(piece)
    return jnp.stack(placed)


def body(source, lower_coef, upper_coef, chunks=4):
    highest = lax.Precision.HIGHEST
    slab_levels, slab_rows, full_x = source.shape
    col_count = lax.axis_size("col")
    row_count = lax.axis_size("row")
    full_y = slab_rows * col_count
    part_x = full_x // col_count
    part_y = full_y // row_count
    chunk_x = part_x // chunks
    index_x = np.arange(full_x)
    table_y = cas_constant(np.arange(full_y), np.arange(full_y), full_y)
    forward_y = table_y.reshape(col_count, slab_rows, row_count, part_y)
    inverse_y = table_y.reshape(row_count, part_y, col_count, slab_rows)
    scale = 1.0 / (full_x * full_y)
    wave_y = lax.axis_index("row") * part_y + lax.iota(jnp.int32, part_y)

    def chunk_waves(chunk):
        return (np.arange(col_count)[:, None] * part_x + chunk * chunk_x
                + np.arange(chunk_x)[None, :]).reshape(-1)

    def along_x(chunk, slab):
        table_chunk = cas_constant(index_x, chunk_waves(chunk), full_x).reshape(full_x, col_count, chunk_x)
        spread = jnp.einsum("zyx,xdi->dziy", slab, table_chunk, precision=highest)
        return lax.all_to_all(spread, "col", 0, 0, tiled=True)

    def middle(chunk, gathered):
        spectra = jnp.einsum("sziy,syhj->hzij", gathered, forward_y, precision=highest)
        columns = exchange(spectra, "row")
        columns = columns.reshape(row_count * slab_levels, chunk_x, part_y)
        wave_x = lax.axis_index("col") * part_x + chunk * chunk_x + lax.iota(jnp.int32, chunk_x)
        eigen_sum = eigen_values(wave_x, full_x)[:, None] + eigen_values(wave_y, full_y)[None, :]
        pinned = (wave_x == 0)[:, None] & (wave_y == 0)[None, :]
        solved = vertical_solve(columns, lower_coef, upper_coef, eigen_sum, pinned)
        solved = solved.reshape(row_count, slab_levels, chunk_x, part_y)
        returned = exchange(solved, "row")
        return jnp.einsum("hzij,hjsy->sziy", returned, inverse_y, precision=highest)

    def back_x(chunk, back_y):
        table_back = cas_constant(chunk_waves(chunk), index_x, full_x).reshape(col_count, chunk_x, full_x)
        scattered = lax.all_to_all(back_y, "col", 0, 0, tiled=True)
        return jnp.einsum("dziy,din->zyn", scattered, table_back, precision=highest)

    gathered = along_x(0, source)
    gathered, source = lax.optimization_barrier((gathered, source))
    pressure = None
    back_y = None
    for chunk in range(chunks):
        gathered_next = along_x(chunk + 1, source) if chunk + 1 < chunks else None
        if back_y is not None:
            part = back_x(chunk - 1, back_y)
            pressure = part if pressure is None else pressure + part
        back_y = middle(chunk, gathered)
        gathered = gathered_next
        gathered, back_y, pressure, source = lax.optimization_barrier((gathered, back_y, pressure, source))
    part = back_x(chunks - 1, back_y)
    pressure = part if pressure is None else pressure + part
    return pressure * scale


def solution(mesh):
    placed = (P("row", "col", None), P(), P())
    return jax.shard_map(
        body, mesh=mesh, in_specs=placed, out_specs=P("row", "col", None), check_vma=False
    )
```

```python
import math

import numpy as np

import jax
import jax.numpy as jnp
from jax import lax
from jax.sharding import PartitionSpec as P
from jax.experimental import pallas as pl
from jax.experimental.pallas import tpu as pltpu


def cas_table(row_index, col_index, length):
    product = row_index[:, None] * col_index[None, :] % length
    angles = product.astype(jnp.float32) * (2.0 * math.pi / length)
    return jnp.cos(angles) + jnp.sin(angles)


def cas_constant(row_index, col_index, length):
    product = np.outer(row_index, col_index) % length
    angles = product.astype(np.float64) * (2.0 * math.pi / length)
    return jnp.asarray((np.cos(angles) + np.sin(angles)).astype(np.float32))


def eigen_values(wave_index, length):
    return 2.0 * jnp.cos(wave_index.astype(jnp.float32) * (2.0 * math.pi / length)) - 2.0


def solve_kernel(lower_ref, upper_ref, eigen_ref, pinned_ref, spectra_ref, solved_ref, ratio_ref):
    levels = spectra_ref.shape[0]
    eigen_sum = eigen_ref[...]
    pinned = pinned_ref[...] > 0.5
    above_first = upper_ref[0]
    head_diag = jnp.where(pinned, 1.0, eigen_sum - above_first)
    head_upper = jnp.where(pinned, 0.0, above_first)
    head_right = jnp.where(pinned, 0.0, spectra_ref[0])
    ratio_ref[0] = head_upper / head_diag
    solved_ref[0] = head_right / head_diag

    def forward(level, carry):
        ratio_before, value_before = carry
        low_coef = lower_ref[level]
        high_coef = jnp.where(level < levels - 1, upper_ref[level], 0.0)
        pivot = eigen_sum - low_coef - high_coef - low_coef * ratio_before
        ratio_next = high_coef / pivot
        value_next = (spectra_ref[level] - low_coef * value_before) / pivot
        ratio_ref[level] = ratio_next
        solved_ref[level] = value_next
        return ratio_next, value_next

    unused, last = lax.fori_loop(1, levels, forward, (ratio_ref[0], solved_ref[0]))

    def backward(step, later):
        level = levels - 2 - step
        result = solved_ref[level] - ratio_ref[level] * later
        solved_ref[level] = result
        return result

    lax.fori_loop(0, levels - 1, backward, last)


def vertical_solve(spectra, lower_coef, upper_coef, eigen_sum, pinned):
    levels, part_x, part_y = spectra.shape
    block = 8 if part_x % 8 == 0 else part_x
    column_spec = pl.BlockSpec((levels, block, part_y), lambda i: (0, i, 0))
    plane_spec = pl.BlockSpec((block, part_y), lambda i: (i, 0))
    scalar_spec = pl.BlockSpec(memory_space=pltpu.SMEM)
    return pl.pallas_call(
        solve_kernel,
        grid=(part_x // block,),
        in_specs=[scalar_spec, scalar_spec, plane_spec, plane_spec, column_spec],
        out_specs=column_spec,
        out_shape=jax.ShapeDtypeStruct(spectra.shape, jnp.float32),
        scratch_shapes=[pltpu.VMEM((levels, block, part_y), jnp.float32)],
    )(lower_coef, upper_coef, eigen_sum, pinned.astype(jnp.float32), spectra)


def exchange(pieces, axis_name):
    count = pieces.shape[0]
    here = lax.axis_index(axis_name)
    arrived = [lax.dynamic_index_in_dim(pieces, here, keepdims=False)]
    for shift in range(1, count):
        outgoing = lax.dynamic_index_in_dim(pieces, (here + shift) % count, keepdims=False)
        perm = [(device, (device + shift) % count) for device in range(count)]
        arrived.append(lax.ppermute(outgoing, axis_name, perm))
    placed = []
    for source in range(count):
        distance = (here - source) % count
        piece = arrived[0]
        for shift in range(1, count):
            piece = jnp.where(distance == shift, arrived[shift], piece)
        placed.append(piece)
    return jnp.stack(placed)


def body(source, lower_coef, upper_coef, chunks=4):
    highest = lax.Precision.HIGHEST
    slab_levels, slab_rows, full_x = source.shape
    col_count = lax.axis_size("col")
    row_count = lax.axis_size("row")
    full_y = slab_rows * col_count
    part_x = full_x // col_count
    part_y = full_y // row_count
    chunk_x = part_x // chunks
    index_x = np.arange(full_x)
    table_y = cas_constant(np.arange(full_y), np.arange(full_y), full_y)
    forward_y = table_y.reshape(col_count, slab_rows, row_count, part_y)
    inverse_y = table_y.reshape(row_count, part_y, col_count, slab_rows)
    scale = 1.0 / (full_x * full_y)
    wave_y = lax.axis_index("row") * part_y + lax.iota(jnp.int32, part_y)

    def chunk_waves(chunk):
        return (np.arange(col_count)[:, None] * part_x + chunk * chunk_x
                + np.arange(chunk_x)[None, :]).reshape(-1)

    def along_x(chunk, slab):
        table_chunk = cas_constant(index_x, chunk_waves(chunk), full_x).reshape(full_x, col_count, chunk_x)
        spread = jnp.einsum("zyx,xdi->dziy", slab, table_chunk, precision=highest)
        return lax.all_to_all(spread, "col", 0, 0, tiled=True)

    def middle(chunk, gathered):
        spectra = jnp.einsum("sziy,syhj->hzij", gathered, forward_y, precision=highest)
        columns = exchange(spectra, "row")
        columns = columns.reshape(row_count * slab_levels, chunk_x, part_y)
        wave_x = lax.axis_index("col") * part_x + chunk * chunk_x + lax.iota(jnp.int32, chunk_x)
        eigen_sum = eigen_values(wave_x, full_x)[:, None] + eigen_values(wave_y, full_y)[None, :]
        pinned = (wave_x == 0)[:, None] & (wave_y == 0)[None, :]
        solved = vertical_solve(columns, lower_coef, upper_coef, eigen_sum, pinned)
        solved = solved.reshape(row_count, slab_levels, chunk_x, part_y)
        returned = exchange(solved, "row")
        return jnp.einsum("hzij,hjsy->sziy", returned, inverse_y, precision=highest)

    def back_x(chunk, back_y):
        table_back = cas_constant(chunk_waves(chunk), index_x, full_x).reshape(col_count, chunk_x, full_x)
        scattered = lax.all_to_all(back_y, "col", 0, 0, tiled=True)
        return jnp.einsum("dziy,din->zyn", scattered, table_back, precision=highest)

    gathered = along_x(0, source)
    pass
    pressure = None
    back_y = None
    for chunk in range(chunks):
        gathered_next = along_x(chunk + 1, source) if chunk + 1 < chunks else None
        if back_y is not None:
            part = back_x(chunk - 1, back_y)
            pressure = part if pressure is None else pressure + part
        back_y = middle(chunk, gathered)
        gathered = gathered_next
        pass
    part = back_x(chunks - 1, back_y)
    pressure = part if pressure is None else pressure + part
    return pressure * scale


def solution(mesh):
    placed = (P("row", "col", None), P(), P())
    return jax.shard_map(
        body, mesh=mesh, in_specs=placed, out_specs=P("row", "col", None), check_vma=False
    )
```

```python
import math

import numpy as np

import jax
import jax.numpy as jnp
from jax import lax
from jax.sharding import PartitionSpec as P
from jax.experimental import pallas as pl
from jax.experimental.pallas import tpu as pltpu


def cas_table(row_index, col_index, length):
    product = row_index[:, None] * col_index[None, :] % length
    angles = product.astype(jnp.float32) * (2.0 * math.pi / length)
    return jnp.cos(angles) + jnp.sin(angles)


def cas_constant(row_index, col_index, length):
    product = np.outer(row_index, col_index) % length
    angles = product.astype(np.float64) * (2.0 * math.pi / length)
    return jnp.asarray((np.cos(angles) + np.sin(angles)).astype(np.float32))


def eigen_values(wave_index, length):
    return 2.0 * jnp.cos(wave_index.astype(jnp.float32) * (2.0 * math.pi / length)) - 2.0


def solve_kernel(lower_ref, upper_ref, eigen_ref, pinned_ref, spectra_ref, solved_ref, ratio_ref):
    levels = spectra_ref.shape[0]
    eigen_sum = eigen_ref[...]
    pinned = pinned_ref[...] > 0.5
    above_first = upper_ref[0]
    head_diag = jnp.where(pinned, 1.0, eigen_sum - above_first)
    head_upper = jnp.where(pinned, 0.0, above_first)
    head_right = jnp.where(pinned, 0.0, spectra_ref[0])
    ratio_ref[0] = head_upper / head_diag
    solved_ref[0] = head_right / head_diag

    def forward(level, carry):
        ratio_before, value_before = carry
        low_coef = lower_ref[level]
        high_coef = jnp.where(level < levels - 1, upper_ref[level], 0.0)
        pivot = eigen_sum - low_coef - high_coef - low_coef * ratio_before
        ratio_next = high_coef / pivot
        value_next = (spectra_ref[level] - low_coef * value_before) / pivot
        ratio_ref[level] = ratio_next
        solved_ref[level] = value_next
        return ratio_next, value_next

    unused, last = lax.fori_loop(1, levels, forward, (ratio_ref[0], solved_ref[0]))

    def backward(step, later):
        level = levels - 2 - step
        result = solved_ref[level] - ratio_ref[level] * later
        solved_ref[level] = result
        return result

    lax.fori_loop(0, levels - 1, backward, last)


def vertical_solve(spectra, lower_coef, upper_coef, eigen_sum, pinned):
    levels, part_x, part_y = spectra.shape
    block = 8 if part_x % 8 == 0 else part_x
    column_spec = pl.BlockSpec((levels, block, part_y), lambda i: (0, i, 0))
    plane_spec = pl.BlockSpec((block, part_y), lambda i: (i, 0))
    scalar_spec = pl.BlockSpec(memory_space=pltpu.SMEM)
    return pl.pallas_call(
        solve_kernel,
        grid=(part_x // block,),
        in_specs=[scalar_spec, scalar_spec, plane_spec, plane_spec, column_spec],
        out_specs=column_spec,
        out_shape=jax.ShapeDtypeStruct(spectra.shape, jnp.float32),
        scratch_shapes=[pltpu.VMEM((levels, block, part_y), jnp.float32)],
    )(lower_coef, upper_coef, eigen_sum, pinned.astype(jnp.float32), spectra)


def exchange(pieces, axis_name):
    count = pieces.shape[0]
    here = lax.axis_index(axis_name)
    arrived = [lax.dynamic_index_in_dim(pieces, here, keepdims=False)]
    for shift in range(1, count):
        outgoing = lax.dynamic_index_in_dim(pieces, (here + shift) % count, keepdims=False)
        perm = [(device, (device + shift) % count) for device in range(count)]
        arrived.append(lax.ppermute(outgoing, axis_name, perm))
    placed = []
    for source in range(count):
        distance = (here - source) % count
        piece = arrived[0]
        for shift in range(1, count):
            piece = jnp.where(distance == shift, arrived[shift], piece)
        placed.append(piece)
    return jnp.stack(placed)


def body(source, lower_coef, upper_coef, chunks=4):
    highest = lax.Precision.HIGHEST
    slab_levels, slab_rows, full_x = source.shape
    col_count = lax.axis_size("col")
    row_count = lax.axis_size("row")
    full_y = slab_rows * col_count
    part_x = full_x // col_count
    part_y = full_y // row_count
    chunk_x = part_x // chunks
    index_x = np.arange(full_x)
    table_y = cas_constant(np.arange(full_y), np.arange(full_y), full_y)
    forward_y = table_y.reshape(col_count, slab_rows, row_count, part_y)
    inverse_y = table_y.reshape(row_count, part_y, col_count, slab_rows)
    scale = 1.0 / (full_x * full_y)
    wave_y = lax.axis_index("row") * part_y + lax.iota(jnp.int32, part_y)

    def chunk_waves(chunk):
        return (np.arange(col_count)[:, None] * part_x + chunk * chunk_x
                + np.arange(chunk_x)[None, :]).reshape(-1)

    def spread_x(chunk):
        table_chunk = cas_constant(index_x, chunk_waves(chunk), full_x).reshape(full_x, col_count, chunk_x)
        return jnp.einsum("zyx,xdi->dziy", source, table_chunk, precision=highest)

    def spectra_y(gathered):
        return jnp.einsum("sziy,syhj->hzij", gathered, forward_y, precision=highest)

    def middle(chunk, spectra):
        columns = exchange(spectra, "row")
        columns = columns.reshape(row_count * slab_levels, chunk_x, part_y)
        wave_x = lax.axis_index("col") * part_x + chunk * chunk_x + lax.iota(jnp.int32, chunk_x)
        eigen_sum = eigen_values(wave_x, full_x)[:, None] + eigen_values(wave_y, full_y)[None, :]
        pinned = (wave_x == 0)[:, None] & (wave_y == 0)[None, :]
        solved = vertical_solve(columns, lower_coef, upper_coef, eigen_sum, pinned)
        solved = solved.reshape(row_count, slab_levels, chunk_x, part_y)
        returned = exchange(solved, "row")
        return jnp.einsum("hzij,hjsy->sziy", returned, inverse_y, precision=highest)

    def back_x(chunk, back_y):
        table_back = cas_constant(chunk_waves(chunk), index_x, full_x).reshape(col_count, chunk_x, full_x)
        scattered = lax.all_to_all(back_y, "col", 0, 0, tiled=True)
        return jnp.einsum("dziy,din->zyn", scattered, table_back, precision=highest)

    lead = min(2, chunks)
    gathered = [lax.all_to_all(spread_x(chunk), "col", 0, 0, tiled=True) for chunk in range(lead)]
    pressure = None
    for chunk in range(chunks):
        spectra = spectra_y(gathered[chunk])
        if chunk + lead < chunks:
            spread, spectra = lax.optimization_barrier((spread_x(chunk + lead), spectra))
            gathered.append(lax.all_to_all(spread, "col", 0, 0, tiled=True))
        part = back_x(chunk, middle(chunk, spectra))
        pressure = part if pressure is None else pressure + part
    return pressure * scale


def solution(mesh):
    placed = (P("row", "col", None), P(), P())
    return jax.shard_map(
        body, mesh=mesh, in_specs=placed, out_specs=P("row", "col", None), check_vma=False
    )
```

```python
import math

import numpy as np

import jax
import jax.numpy as jnp
from jax import lax
from jax.sharding import PartitionSpec as P
from jax.experimental import pallas as pl
from jax.experimental.pallas import tpu as pltpu


def cas_table(row_index, col_index, length):
    product = row_index[:, None] * col_index[None, :] % length
    angles = product.astype(jnp.float32) * (2.0 * math.pi / length)
    return jnp.cos(angles) + jnp.sin(angles)


def cas_constant(row_index, col_index, length):
    product = np.outer(row_index, col_index) % length
    angles = product.astype(np.float64) * (2.0 * math.pi / length)
    return jnp.asarray((np.cos(angles) + np.sin(angles)).astype(np.float32))


def eigen_values(wave_index, length):
    return 2.0 * jnp.cos(wave_index.astype(jnp.float32) * (2.0 * math.pi / length)) - 2.0


def solve_kernel(lower_ref, upper_ref, eigen_ref, pinned_ref, spectra_ref, solved_ref, ratio_ref):
    levels = spectra_ref.shape[0]
    eigen_sum = eigen_ref[...]
    pinned = pinned_ref[...] > 0.5
    above_first = upper_ref[0]
    head_diag = jnp.where(pinned, 1.0, eigen_sum - above_first)
    head_upper = jnp.where(pinned, 0.0, above_first)
    head_right = jnp.where(pinned, 0.0, spectra_ref[0])
    ratio_ref[0] = head_upper / head_diag
    solved_ref[0] = head_right / head_diag

    def forward(level, carry):
        ratio_before, value_before = carry
        low_coef = lower_ref[level]
        high_coef = jnp.where(level < levels - 1, upper_ref[level], 0.0)
        pivot = eigen_sum - low_coef - high_coef - low_coef * ratio_before
        ratio_next = high_coef / pivot
        value_next = (spectra_ref[level] - low_coef * value_before) / pivot
        ratio_ref[level] = ratio_next
        solved_ref[level] = value_next
        return ratio_next, value_next

    unused, last = lax.fori_loop(1, levels, forward, (ratio_ref[0], solved_ref[0]))

    def backward(step, later):
        level = levels - 2 - step
        result = solved_ref[level] - ratio_ref[level] * later
        solved_ref[level] = result
        return result

    lax.fori_loop(0, levels - 1, backward, last)


def vertical_solve(spectra, lower_coef, upper_coef, eigen_sum, pinned):
    levels, part_x, part_y = spectra.shape
    block = 8 if part_x % 8 == 0 else part_x
    column_spec = pl.BlockSpec((levels, block, part_y), lambda i: (0, i, 0))
    plane_spec = pl.BlockSpec((block, part_y), lambda i: (i, 0))
    scalar_spec = pl.BlockSpec(memory_space=pltpu.SMEM)
    return pl.pallas_call(
        solve_kernel,
        grid=(part_x // block,),
        in_specs=[scalar_spec, scalar_spec, plane_spec, plane_spec, column_spec],
        out_specs=column_spec,
        out_shape=jax.ShapeDtypeStruct(spectra.shape, jnp.float32),
        scratch_shapes=[pltpu.VMEM((levels, block, part_y), jnp.float32)],
    )(lower_coef, upper_coef, eigen_sum, pinned.astype(jnp.float32), spectra)


def exchange(pieces, axis_name):
    count = pieces.shape[0]
    here = lax.axis_index(axis_name)
    arrived = [lax.dynamic_index_in_dim(pieces, here, keepdims=False)]
    for shift in range(1, count):
        outgoing = lax.dynamic_index_in_dim(pieces, (here + shift) % count, keepdims=False)
        perm = [(device, (device + shift) % count) for device in range(count)]
        arrived.append(lax.ppermute(outgoing, axis_name, perm))
    placed = []
    for source in range(count):
        distance = (here - source) % count
        piece = arrived[0]
        for shift in range(1, count):
            piece = jnp.where(distance == shift, arrived[shift], piece)
        placed.append(piece)
    return jnp.stack(placed)


def body(source, lower_coef, upper_coef, chunks=4):
    highest = lax.Precision.HIGHEST
    slab_levels, slab_rows, full_x = source.shape
    col_count = lax.axis_size("col")
    row_count = lax.axis_size("row")
    full_y = slab_rows * col_count
    part_x = full_x // col_count
    part_y = full_y // row_count
    chunk_x = part_x // chunks
    index_x = np.arange(full_x)
    table_y = cas_constant(np.arange(full_y), np.arange(full_y), full_y)
    forward_y = table_y.reshape(col_count, slab_rows, row_count, part_y)
    inverse_y = table_y.reshape(row_count, part_y, col_count, slab_rows)
    scale = 1.0 / (full_x * full_y)
    wave_y = lax.axis_index("row") * part_y + lax.iota(jnp.int32, part_y)

    def chunk_waves(chunk):
        return (np.arange(col_count)[:, None] * part_x + chunk * chunk_x
                + np.arange(chunk_x)[None, :]).reshape(-1)

    def spread_x(chunk):
        table_chunk = cas_constant(index_x, chunk_waves(chunk), full_x).reshape(full_x, col_count, chunk_x)
        return jnp.einsum("zyx,xdi->dziy", source, table_chunk, precision=highest)

    def spectra_y(gathered):
        return jnp.einsum("sziy,syhj->hzij", gathered, forward_y, precision=highest)

    def middle(chunk, spectra):
        columns = exchange(spectra, "row")
        columns = columns.reshape(row_count * slab_levels, chunk_x, part_y)
        wave_x = lax.axis_index("col") * part_x + chunk * chunk_x + lax.iota(jnp.int32, chunk_x)
        eigen_sum = eigen_values(wave_x, full_x)[:, None] + eigen_values(wave_y, full_y)[None, :]
        pinned = (wave_x == 0)[:, None] & (wave_y == 0)[None, :]
        solved = vertical_solve(columns, lower_coef, upper_coef, eigen_sum, pinned)
        solved = solved.reshape(row_count, slab_levels, chunk_x, part_y)
        returned = exchange(solved, "row")
        return jnp.einsum("hzij,hjsy->sziy", returned, inverse_y, precision=lax.Precision.HIGH)

    def back_x(chunk, back_y):
        table_back = cas_constant(chunk_waves(chunk), index_x, full_x).reshape(col_count, chunk_x, full_x)
        scattered = lax.all_to_all(back_y, "col", 0, 0, tiled=True)
        return jnp.einsum("dziy,din->zyn", scattered, table_back, precision=lax.Precision.HIGH)

    lead = min(2, chunks)
    gathered = [lax.all_to_all(spread_x(chunk), "col", 0, 0, tiled=True) for chunk in range(lead)]
    pressure = None
    for chunk in range(chunks):
        spectra = spectra_y(gathered[chunk])
        if chunk + lead < chunks:
            spread, spectra = lax.optimization_barrier((spread_x(chunk + lead), spectra))
            gathered.append(lax.all_to_all(spread, "col", 0, 0, tiled=True))
        part = back_x(chunk, middle(chunk, spectra))
        pressure = part if pressure is None else pressure + part
    return pressure * scale


def solution(mesh):
    placed = (P("row", "col", None), P(), P())
    return jax.shard_map(
        body, mesh=mesh, in_specs=placed, out_specs=P("row", "col", None), check_vma=False
    )
```

```python
import math

import numpy as np

import jax
import jax.numpy as jnp
from jax import lax
from jax.sharding import PartitionSpec as P
from jax.experimental import pallas as pl
from jax.experimental.pallas import tpu as pltpu


def cas_table(row_index, col_index, length):
    product = row_index[:, None] * col_index[None, :] % length
    angles = product.astype(jnp.float32) * (2.0 * math.pi / length)
    return jnp.cos(angles) + jnp.sin(angles)


def cas_constant(row_index, col_index, length):
    product = np.outer(row_index, col_index) % length
    angles = product.astype(np.float64) * (2.0 * math.pi / length)
    return jnp.asarray((np.cos(angles) + np.sin(angles)).astype(np.float32))


def eigen_values(wave_index, length):
    return 2.0 * jnp.cos(wave_index.astype(jnp.float32) * (2.0 * math.pi / length)) - 2.0


def solve_kernel(lower_ref, upper_ref, eigen_ref, pinned_ref, spectra_ref, solved_ref, ratio_ref):
    levels = spectra_ref.shape[0]
    eigen_sum = eigen_ref[...]
    pinned = pinned_ref[...] > 0.5
    above_first = upper_ref[0]
    head_diag = jnp.where(pinned, 1.0, eigen_sum - above_first)
    head_upper = jnp.where(pinned, 0.0, above_first)
    head_right = jnp.where(pinned, 0.0, spectra_ref[0])
    ratio_ref[0] = head_upper / head_diag
    solved_ref[0] = head_right / head_diag

    def forward(level, carry):
        ratio_before, value_before = carry
        low_coef = lower_ref[level]
        high_coef = jnp.where(level < levels - 1, upper_ref[level], 0.0)
        pivot = eigen_sum - low_coef - high_coef - low_coef * ratio_before
        ratio_next = high_coef / pivot
        value_next = (spectra_ref[level] - low_coef * value_before) / pivot
        ratio_ref[level] = ratio_next
        solved_ref[level] = value_next
        return ratio_next, value_next

    unused, last = lax.fori_loop(1, levels, forward, (ratio_ref[0], solved_ref[0]))

    def backward(step, later):
        level = levels - 2 - step
        result = solved_ref[level] - ratio_ref[level] * later
        solved_ref[level] = result
        return result

    lax.fori_loop(0, levels - 1, backward, last)


def vertical_solve(spectra, lower_coef, upper_coef, eigen_sum, pinned):
    levels, part_x, part_y = spectra.shape
    block = 8 if part_x % 8 == 0 else part_x
    column_spec = pl.BlockSpec((levels, block, part_y), lambda i: (0, i, 0))
    plane_spec = pl.BlockSpec((block, part_y), lambda i: (i, 0))
    scalar_spec = pl.BlockSpec(memory_space=pltpu.SMEM)
    return pl.pallas_call(
        solve_kernel,
        grid=(part_x // block,),
        in_specs=[scalar_spec, scalar_spec, plane_spec, plane_spec, column_spec],
        out_specs=column_spec,
        out_shape=jax.ShapeDtypeStruct(spectra.shape, jnp.float32),
        scratch_shapes=[pltpu.VMEM((levels, block, part_y), jnp.float32)],
    )(lower_coef, upper_coef, eigen_sum, pinned.astype(jnp.float32), spectra)


def exchange(pieces, axis_name):
    count = pieces.shape[0]
    here = lax.axis_index(axis_name)
    arrived = [lax.dynamic_index_in_dim(pieces, here, keepdims=False)]
    for shift in range(1, count):
        outgoing = lax.dynamic_index_in_dim(pieces, (here + shift) % count, keepdims=False)
        perm = [(device, (device + shift) % count) for device in range(count)]
        arrived.append(lax.ppermute(outgoing, axis_name, perm))
    placed = []
    for source in range(count):
        distance = (here - source) % count
        piece = arrived[0]
        for shift in range(1, count):
            piece = jnp.where(distance == shift, arrived[shift], piece)
        placed.append(piece)
    return jnp.stack(placed)


def body(source, lower_coef, upper_coef, chunks=6):
    highest = lax.Precision.HIGHEST
    slab_levels, slab_rows, full_x = source.shape
    col_count = lax.axis_size("col")
    row_count = lax.axis_size("row")
    full_y = slab_rows * col_count
    part_x = full_x // col_count
    part_y = full_y // row_count
    chunk_x = part_x // chunks
    index_x = np.arange(full_x)
    table_y = cas_constant(np.arange(full_y), np.arange(full_y), full_y)
    forward_y = table_y.reshape(col_count, slab_rows, row_count, part_y)
    inverse_y = table_y.reshape(row_count, part_y, col_count, slab_rows)
    scale = 1.0 / (full_x * full_y)
    wave_y = lax.axis_index("row") * part_y + lax.iota(jnp.int32, part_y)

    def chunk_waves(chunk):
        return (np.arange(col_count)[:, None] * part_x + chunk * chunk_x
                + np.arange(chunk_x)[None, :]).reshape(-1)

    def spread_x(chunk):
        table_chunk = cas_constant(index_x, chunk_waves(chunk), full_x).reshape(full_x, col_count, chunk_x)
        return jnp.einsum("zyx,xdi->dziy", source, table_chunk, precision=highest)

    def spectra_y(gathered):
        return jnp.einsum("sziy,syhj->hzij", gathered, forward_y, precision=highest)

    def middle(chunk, spectra):
        columns = exchange(spectra, "row")
        columns = columns.reshape(row_count * slab_levels, chunk_x, part_y)
        wave_x = lax.axis_index("col") * part_x + chunk * chunk_x + lax.iota(jnp.int32, chunk_x)
        eigen_sum = eigen_values(wave_x, full_x)[:, None] + eigen_values(wave_y, full_y)[None, :]
        pinned = (wave_x == 0)[:, None] & (wave_y == 0)[None, :]
        solved = vertical_solve(columns, lower_coef, upper_coef, eigen_sum, pinned)
        solved = solved.reshape(row_count, slab_levels, chunk_x, part_y)
        returned = exchange(solved, "row")
        return jnp.einsum("hzij,hjsy->sziy", returned, inverse_y, precision=lax.Precision.HIGH)

    def back_x(chunk, back_y):
        table_back = cas_constant(chunk_waves(chunk), index_x, full_x).reshape(col_count, chunk_x, full_x)
        scattered = lax.all_to_all(back_y, "col", 0, 0, tiled=True)
        return jnp.einsum("dziy,din->zyn", scattered, table_back, precision=lax.Precision.HIGH)

    lead = min(2, chunks)
    gathered = [lax.all_to_all(spread_x(chunk), "col", 0, 0, tiled=True) for chunk in range(lead)]
    pressure = None
    for chunk in range(chunks):
        spectra = spectra_y(gathered[chunk])
        if chunk + lead < chunks:
            spread, spectra = lax.optimization_barrier((spread_x(chunk + lead), spectra))
            gathered.append(lax.all_to_all(spread, "col", 0, 0, tiled=True))
        part = back_x(chunk, middle(chunk, spectra))
        pressure = part if pressure is None else pressure + part
    return pressure * scale


def solution(mesh):
    placed = (P("row", "col", None), P(), P())
    return jax.shard_map(
        body, mesh=mesh, in_specs=placed, out_specs=P("row", "col", None), check_vma=False
    )
```

```python
import math

import numpy as np

import jax
import jax.numpy as jnp
from jax import lax
from jax.sharding import PartitionSpec as P
from jax.experimental import pallas as pl
from jax.experimental.pallas import tpu as pltpu


def cas_table(row_index, col_index, length):
    product = row_index[:, None] * col_index[None, :] % length
    angles = product.astype(jnp.float32) * (2.0 * math.pi / length)
    return jnp.cos(angles) + jnp.sin(angles)


def cas_constant(row_index, col_index, length):
    product = np.outer(row_index, col_index) % length
    angles = product.astype(np.float64) * (2.0 * math.pi / length)
    return jnp.asarray((np.cos(angles) + np.sin(angles)).astype(np.float32))


def eigen_values(wave_index, length):
    return 2.0 * jnp.cos(wave_index.astype(jnp.float32) * (2.0 * math.pi / length)) - 2.0


def solve_kernel(lower_ref, upper_ref, eigen_ref, pinned_ref, spectra_ref, solved_ref, ratio_ref):
    levels = spectra_ref.shape[0]
    eigen_sum = eigen_ref[...]
    pinned = pinned_ref[...] > 0.5
    above_first = upper_ref[0]
    head_diag = jnp.where(pinned, 1.0, eigen_sum - above_first)
    head_upper = jnp.where(pinned, 0.0, above_first)
    head_right = jnp.where(pinned, 0.0, spectra_ref[0])
    ratio_ref[0] = head_upper / head_diag
    solved_ref[0] = head_right / head_diag

    def forward(level, carry):
        ratio_before, value_before = carry
        low_coef = lower_ref[level]
        high_coef = jnp.where(level < levels - 1, upper_ref[level], 0.0)
        pivot = eigen_sum - low_coef - high_coef - low_coef * ratio_before
        ratio_next = high_coef / pivot
        value_next = (spectra_ref[level] - low_coef * value_before) / pivot
        ratio_ref[level] = ratio_next
        solved_ref[level] = value_next
        return ratio_next, value_next

    unused, last = lax.fori_loop(1, levels, forward, (ratio_ref[0], solved_ref[0]))

    def backward(step, later):
        level = levels - 2 - step
        result = solved_ref[level] - ratio_ref[level] * later
        solved_ref[level] = result
        return result

    lax.fori_loop(0, levels - 1, backward, last)


def vertical_solve(spectra, lower_coef, upper_coef, eigen_sum, pinned):
    levels, part_x, part_y = spectra.shape
    block = 8 if part_x % 8 == 0 else part_x
    column_spec = pl.BlockSpec((levels, block, part_y), lambda i: (0, i, 0))
    plane_spec = pl.BlockSpec((block, part_y), lambda i: (i, 0))
    scalar_spec = pl.BlockSpec(memory_space=pltpu.SMEM)
    return pl.pallas_call(
        solve_kernel,
        grid=(part_x // block,),
        in_specs=[scalar_spec, scalar_spec, plane_spec, plane_spec, column_spec],
        out_specs=column_spec,
        out_shape=jax.ShapeDtypeStruct(spectra.shape, jnp.float32),
        scratch_shapes=[pltpu.VMEM((levels, block, part_y), jnp.float32)],
    )(lower_coef, upper_coef, eigen_sum, pinned.astype(jnp.float32), spectra)


def exchange(pieces, axis_name):
    count = pieces.shape[0]
    here = lax.axis_index(axis_name)
    arrived = [lax.dynamic_index_in_dim(pieces, here, keepdims=False)]
    for shift in range(1, count):
        outgoing = lax.dynamic_index_in_dim(pieces, (here + shift) % count, keepdims=False)
        perm = [(device, (device + shift) % count) for device in range(count)]
        arrived.append(lax.ppermute(outgoing, axis_name, perm))
    placed = []
    for source in range(count):
        distance = (here - source) % count
        piece = arrived[0]
        for shift in range(1, count):
            piece = jnp.where(distance == shift, arrived[shift], piece)
        placed.append(piece)
    return jnp.stack(placed)


def body(source, lower_coef, upper_coef, chunks=4):
    highest = lax.Precision.HIGHEST
    slab_levels, slab_rows, full_x = source.shape
    col_count = lax.axis_size("col")
    row_count = lax.axis_size("row")
    full_y = slab_rows * col_count
    part_x = full_x // col_count
    part_y = full_y // row_count
    chunk_x = part_x // chunks
    index_x = np.arange(full_x)
    table_y = cas_constant(np.arange(full_y), np.arange(full_y), full_y)
    forward_y = table_y.reshape(col_count, slab_rows, row_count, part_y)
    inverse_y = table_y.reshape(row_count, part_y, col_count, slab_rows)
    scale = 1.0 / (full_x * full_y)
    wave_y = lax.axis_index("row") * part_y + lax.iota(jnp.int32, part_y)

    def chunk_waves(chunk):
        return (np.arange(col_count)[:, None] * part_x + chunk * chunk_x
                + np.arange(chunk_x)[None, :]).reshape(-1)

    def spread_x(chunk):
        table_chunk = cas_constant(index_x, chunk_waves(chunk), full_x).reshape(full_x, col_count, chunk_x)
        return jnp.einsum("zyx,xdi->dziy", source, table_chunk, precision=highest)

    def spectra_y(gathered):
        return jnp.einsum("sziy,syhj->hzij", gathered, forward_y, precision=highest)

    def middle(chunk, spectra):
        columns = exchange(spectra, "row")
        columns = columns.reshape(row_count * slab_levels, chunk_x, part_y)
        wave_x = lax.axis_index("col") * part_x + chunk * chunk_x + lax.iota(jnp.int32, chunk_x)
        eigen_sum = eigen_values(wave_x, full_x)[:, None] + eigen_values(wave_y, full_y)[None, :]
        pinned = (wave_x == 0)[:, None] & (wave_y == 0)[None, :]
        solved = vertical_solve(columns, lower_coef, upper_coef, eigen_sum, pinned)
        solved = solved.reshape(row_count, slab_levels, chunk_x, part_y)
        returned = exchange(solved, "row")
        return jnp.einsum("hzij,hjsy->sziy", returned, inverse_y, precision=lax.Precision.HIGH)

    def back_x(chunk, back_y):
        table_back = cas_constant(chunk_waves(chunk), index_x, full_x).reshape(col_count, chunk_x, full_x)
        scattered = lax.all_to_all(back_y, "col", 0, 0, tiled=True)
        return jnp.einsum("dziy,din->zyn", scattered, table_back, precision=lax.Precision.HIGH)

    lead = min(2, chunks)
    gathered = [lax.all_to_all(spread_x(chunk), "col", 0, 0, tiled=True) for chunk in range(lead)]
    pressure = None
    for chunk in range(chunks):
        spectra = spectra_y(gathered[chunk])
        if chunk + lead < chunks:
            spread, spectra = lax.optimization_barrier((spread_x(chunk + lead), spectra))
            gathered.append(lax.all_to_all(spread, "col", 0, 0, tiled=True))
        part = back_x(chunk, middle(chunk, spectra))
        pressure = part if pressure is None else pressure + part
        if chunk + 1 < chunks:
            pressure = lax.optimization_barrier(pressure)
    return pressure * scale


def solution(mesh):
    placed = (P("row", "col", None), P(), P())
    return jax.shard_map(
        body, mesh=mesh, in_specs=placed, out_specs=P("row", "col", None), check_vma=False
    )
```

```python
import math

import numpy as np

import jax
import jax.numpy as jnp
from jax import lax
from jax.sharding import PartitionSpec as P
from jax.experimental import pallas as pl
from jax.experimental.pallas import tpu as pltpu


def cas_table(row_index, col_index, length):
    product = row_index[:, None] * col_index[None, :] % length
    angles = product.astype(jnp.float32) * (2.0 * math.pi / length)
    return jnp.cos(angles) + jnp.sin(angles)


def cas_constant(row_index, col_index, length, factor=1.0):
    product = np.outer(row_index, col_index) % length
    angles = product.astype(np.float64) * (2.0 * math.pi / length)
    return jnp.asarray(((np.cos(angles) + np.sin(angles)) * factor).astype(np.float32))


def eigen_values(wave_index, length):
    return 2.0 * jnp.cos(wave_index.astype(jnp.float32) * (2.0 * math.pi / length)) - 2.0


def solve_kernel(lower_ref, upper_ref, eigen_ref, pinned_ref, spectra_ref, solved_ref, ratio_ref):
    levels = spectra_ref.shape[0]
    eigen_sum = eigen_ref[...]
    pinned = pinned_ref[...] > 0.5
    above_first = upper_ref[0]
    head_diag = jnp.where(pinned, 1.0, eigen_sum - above_first)
    head_upper = jnp.where(pinned, 0.0, above_first)
    head_right = jnp.where(pinned, 0.0, spectra_ref[0])
    ratio_ref[0] = head_upper / head_diag
    solved_ref[0] = head_right / head_diag

    def forward(level, carry):
        ratio_before, value_before = carry
        low_coef = lower_ref[level]
        high_coef = jnp.where(level < levels - 1, upper_ref[level], 0.0)
        pivot = eigen_sum - low_coef - high_coef - low_coef * ratio_before
        ratio_next = high_coef / pivot
        value_next = (spectra_ref[level] - low_coef * value_before) / pivot
        ratio_ref[level] = ratio_next
        solved_ref[level] = value_next
        return ratio_next, value_next

    unused, last = lax.fori_loop(1, levels, forward, (ratio_ref[0], solved_ref[0]))

    def backward(step, later):
        level = levels - 2 - step
        result = solved_ref[level] - ratio_ref[level] * later
        solved_ref[level] = result
        return result

    lax.fori_loop(0, levels - 1, backward, last)


def vertical_solve(spectra, lower_coef, upper_coef, eigen_sum, pinned):
    levels, part_x, part_y = spectra.shape
    block = 8 if part_x % 8 == 0 else part_x
    column_spec = pl.BlockSpec((levels, block, part_y), lambda i: (0, i, 0))
    plane_spec = pl.BlockSpec((block, part_y), lambda i: (i, 0))
    scalar_spec = pl.BlockSpec(memory_space=pltpu.SMEM)
    return pl.pallas_call(
        solve_kernel,
        grid=(part_x // block,),
        in_specs=[scalar_spec, scalar_spec, plane_spec, plane_spec, column_spec],
        out_specs=column_spec,
        out_shape=jax.ShapeDtypeStruct(spectra.shape, jnp.float32),
        scratch_shapes=[pltpu.VMEM((levels, block, part_y), jnp.float32)],
    )(lower_coef, upper_coef, eigen_sum, pinned.astype(jnp.float32), spectra)


def exchange(pieces, axis_name):
    count = pieces.shape[0]
    here = lax.axis_index(axis_name)
    arrived = [lax.dynamic_index_in_dim(pieces, here, keepdims=False)]
    for shift in range(1, count):
        outgoing = lax.dynamic_index_in_dim(pieces, (here + shift) % count, keepdims=False)
        perm = [(device, (device + shift) % count) for device in range(count)]
        arrived.append(lax.ppermute(outgoing, axis_name, perm))
    placed = []
    for source in range(count):
        distance = (here - source) % count
        piece = arrived[0]
        for shift in range(1, count):
            piece = jnp.where(distance == shift, arrived[shift], piece)
        placed.append(piece)
    return jnp.stack(placed)


def body(source, lower_coef, upper_coef, chunks=4):
    highest = lax.Precision.HIGHEST
    slab_levels, slab_rows, full_x = source.shape
    col_count = lax.axis_size("col")
    row_count = lax.axis_size("row")
    full_y = slab_rows * col_count
    part_x = full_x // col_count
    part_y = full_y // row_count
    chunk_x = part_x // chunks
    index_x = np.arange(full_x)
    table_y = cas_constant(np.arange(full_y), np.arange(full_y), full_y)
    forward_y = table_y.reshape(col_count, slab_rows, row_count, part_y)
    inverse_y = table_y.reshape(row_count, part_y, col_count, slab_rows)
    scale = 1.0 / (full_x * full_y)
    wave_y = lax.axis_index("row") * part_y + lax.iota(jnp.int32, part_y)

    def chunk_waves(chunk):
        return (np.arange(col_count)[:, None] * part_x + chunk * chunk_x
                + np.arange(chunk_x)[None, :]).reshape(-1)

    def spread_x(chunk):
        table_chunk = cas_constant(index_x, chunk_waves(chunk), full_x).reshape(full_x, col_count, chunk_x)
        return jnp.einsum("zyx,xdi->dziy", source, table_chunk, precision=highest)

    def spectra_y(gathered):
        return jnp.einsum("sziy,syhj->hzij", gathered, forward_y, precision=highest)

    def middle(chunk, spectra):
        columns = exchange(spectra, "row")
        columns = columns.reshape(row_count * slab_levels, chunk_x, part_y)
        wave_x = lax.axis_index("col") * part_x + chunk * chunk_x + lax.iota(jnp.int32, chunk_x)
        eigen_sum = eigen_values(wave_x, full_x)[:, None] + eigen_values(wave_y, full_y)[None, :]
        pinned = (wave_x == 0)[:, None] & (wave_y == 0)[None, :]
        solved = vertical_solve(columns, lower_coef, upper_coef, eigen_sum, pinned)
        solved = solved.reshape(row_count, slab_levels, chunk_x, part_y)
        returned = exchange(solved, "row")
        return jnp.einsum("hzij,hjsy->sziy", returned, inverse_y, precision=lax.Precision.HIGH)

    def back_x(chunk, back_y):
        table_back = cas_constant(chunk_waves(chunk), index_x, full_x, scale).reshape(col_count, chunk_x, full_x)
        scattered = lax.all_to_all(back_y, "col", 0, 0, tiled=True)
        return jnp.einsum("dziy,din->zyn", scattered, table_back, precision=lax.Precision.HIGH)

    lead = min(2, chunks)
    gathered = [lax.all_to_all(spread_x(chunk), "col", 0, 0, tiled=True) for chunk in range(lead)]
    pressure = None
    for chunk in range(chunks):
        spectra = spectra_y(gathered[chunk])
        if chunk + lead < chunks:
            spread, spectra = lax.optimization_barrier((spread_x(chunk + lead), spectra))
            gathered.append(lax.all_to_all(spread, "col", 0, 0, tiled=True))
        part = back_x(chunk, middle(chunk, spectra))
        pressure = part if pressure is None else pressure + part
        if chunk + 1 < chunks:
            pressure = lax.optimization_barrier(pressure)
    return pressure


def solution(mesh):
    placed = (P("row", "col", None), P(), P())
    return jax.shard_map(
        body, mesh=mesh, in_specs=placed, out_specs=P("row", "col", None), check_vma=False
    )
```
